256 devices in a mesh: grp: 16 (over y_hi, z), blk: 16 (over x, y_lo, core).
Axes of the slice: x: 4, y: 4 (y_hi: 2, y_lo: 2; y = y_hi * 2 + y_lo), z: 8, core: 2. Of those that a mesh axis runs over, the one named last changes fastest.
Arguments:
- src_codes: int32 [262144, 1024], P(('grp', 'blk')), may hold values from -119 to 119
- src_exps: int32 [262144, 8], P(('grp', 'blk')), may hold values from 0 to 3
- signs: int32 [262144, 256], P(('grp', 'blk')), may hold values from 0 to 1
- tgt_codes: int32 [4096, 1024], P('blk'), may hold values from -119 to 119
- tgt_exps: int32 [4096, 8], P('blk'), may hold values from 0 to 3
Outputs:
- kernel_product: float32 [4096, 256], P('blk', 'grp')
The draws below stay inside these ranges and needn't reach their ends.
All inputs are finite; a program needn't handle non-finite values.
Results may differ from the reference program's by a relative error of at most 0.003.
Values may be sent and summed in bfloat16 or wider, within the bound.
No kernel may reach another device: no remote copies, remote signals or barrier semaphores. Data moves between devices by JAX's collectives and lax.ppermute only.
A program may use at most 64 MiB of HBM per device.

```python
import math
import jax
import jax.numpy as jnp
from jax import lax

D = 1024
QBLOCK = 128
RHS = 256
S_DEV = 1024
TARGETS = 4096
SOURCES = 262144


latent_width = 16


center_reach = 5


nudge_reach = 3


anchor_reach = 28


jitter_reach = 3


code_limit = 119


block_scale = 4


group_rows = 128


def group_tables(key):
    groups = max(SOURCES // group_rows, 1)
    centers = jax.random.randint(jax.random.fold_in(key, 201), (groups, latent_width), -center_reach, center_reach + 1, dtype=jnp.int32)
    anchors = jax.random.randint(jax.random.fold_in(key, 205), (groups, D), -anchor_reach, anchor_reach + 1, dtype=jnp.int32)
    basis = jax.random.randint(jax.random.fold_in(key, 202), (latent_width, D), 0, 2, dtype=jnp.int32) * 2 - 1
    return (groups, centers, anchors, basis)


def quantize_rows(combined, level):
    count = combined.shape[0]
    blocks = D // QBLOCK
    valued = (combined * block_scale).reshape(count, blocks, QBLOCK)
    largest = jnp.max(jnp.abs(valued), axis=2)
    needed = (largest > code_limit).astype(jnp.int32) + (largest > 2 * code_limit).astype(jnp.int32) + (largest > 4 * code_limit).astype(jnp.int32)
    lowered = (level == 0).astype(jnp.int32)
    raised = (level == 3).astype(jnp.int32)
    exponent = jnp.clip(needed - lowered + raised, 0, 3)
    divisor = 1 + (exponent >= 1).astype(jnp.int32) + 2 * (exponent >= 2).astype(jnp.int32) + 4 * (exponent >= 3).astype(jnp.int32)
    code_rows = jnp.clip(jnp.floor_divide(valued, divisor[:, :, None]), -code_limit, code_limit)
    return (code_rows.reshape(count, D), exponent)


def build_points(key, count, salt):
    groups, centers, anchors, basis = group_tables(key)
    chosen = jax.random.randint(jax.random.fold_in(key, salt), (count,), 0, groups, dtype=jnp.int32)
    nudge = jax.random.randint(jax.random.fold_in(key, salt + 1), (count, latent_width), -nudge_reach, nudge_reach + 1, dtype=jnp.int32)
    jitter = jax.random.randint(jax.random.fold_in(key, salt + 2), (count, D), -jitter_reach, jitter_reach + 1, dtype=jnp.int32)
    level = jax.random.randint(jax.random.fold_in(key, salt + 3), (count, D // QBLOCK), 0, 4, dtype=jnp.int32)
    latent = jnp.take(centers, chosen, axis=0) + nudge
    combined = jnp.dot(latent, basis, preferred_element_type=jnp.int32) + jnp.take(anchors, chosen, axis=0) + jitter
    return quantize_rows(combined, level)


def draw_src_codes(key, part):
    return build_points(key, SOURCES, 210)[0]


def draw_src_exps(key, part):
    return build_points(key, SOURCES, 210)[1]


def draw_tgt_codes(key, part):
    return build_points(key, TARGETS, 220)[0]


def draw_tgt_exps(key, part):
    return build_points(key, TARGETS, 220)[1]


def with_ends(values, rng, low, high):
    longest = values.shape.index(max(values.shape))
    spots = []
    for shift in (0, 1):
        where = [jax.random.randint(jax.random.fold_in(rng, axis), (), 0, length) for axis, length in enumerate(values.shape)]
        where[longest] = (where[longest] + shift) % values.shape[longest]
        spots.append(tuple(where))
    return values.at[spots[0]].set(low).at[spots[1]].set(high)


def setup_inputs(seed: int = 0) -> dict:
    key_of = jax.random.split(jax.random.key(seed), 6)
    return {
        "src_codes": draw_src_codes(jax.random.fold_in(key_of[5], 71), 0),
        "src_exps": draw_src_exps(jax.random.fold_in(key_of[5], 71), 0),
        "signs": with_ends(jax.random.randint(key_of[2], (SOURCES, RHS), 0, 2), jax.random.fold_in(key_of[2], 1), 0, 1).astype(jnp.int32),
        "tgt_codes": draw_tgt_codes(jax.random.fold_in(key_of[5], 71), 0),
        "tgt_exps": draw_tgt_exps(jax.random.fold_in(key_of[5], 71), 0),
    }


kernel_rate = 20.0

def dequantize(codes, exponents):
    points, columns = codes.shape
    blocks = exponents.shape[1]
    factor = jnp.zeros(exponents.shape, jnp.float32)
    for level_index in range(4):
        factor = factor + jnp.where(exponents == level_index, 2.0 ** (level_index - 9), 0.0)
    scaled_codes = codes.reshape(points, blocks, columns // blocks).astype(jnp.float32) * factor[:, :, None]
    return scaled_codes.reshape(points, columns).astype(jnp.bfloat16)

def squares(points_bf):
    widened = points_bf.astype(jnp.float32)
    return lax.optimization_barrier(jnp.sum(widened * widened, axis=1))

def kernel_block(targets_bf, sources_bf, source_sq, rhs_values):
    target_sq = squares(targets_bf)
    inner_products = lax.dot_general(targets_bf, sources_bf, (((1,), (1,)), ((), ())), preferred_element_type=jnp.float32)
    squared = target_sq[:, None] + source_sq[None, :] - 2.0 * inner_products
    scaled = kernel_rate * jnp.sqrt(squared) / math.sqrt(targets_bf.shape[1])
    matern = ((1.0 + scaled + scaled * scaled / 3.0) * jnp.exp(-scaled)).astype(jnp.bfloat16)
    return jnp.dot(matern, rhs_values, preferred_element_type=jnp.float32)

def reference(src_codes, src_exps, signs, tgt_codes, tgt_exps):
    sources_bf = dequantize(src_codes, src_exps)
    targets_bf = dequantize(tgt_codes, tgt_exps)
    rhs_values = (2 * signs - 1).astype(jnp.bfloat16)
    source_sq = squares(sources_bf)
    groups = SOURCES // S_DEV
    stacked = (sources_bf.reshape(groups, S_DEV, D), source_sq.reshape(groups, S_DEV), rhs_values.reshape(groups, S_DEV, RHS))

    def advance(running, sliced):
        return (running + kernel_block(targets_bf, sliced[0], sliced[1], sliced[2]), None)
    running, _ = lax.scan(advance, jnp.zeros((TARGETS, RHS), jnp.float32), stacked)
    return running * (4.0 / math.sqrt(SOURCES))
```

```python
import math

import jax
import jax.numpy as jnp
from jax import lax
from jax.sharding import PartitionSpec as P

kernel_rate = 20.0


def shifted(block, axis, distance):
    devices = range(lax.axis_size(axis))
    route = [((i - distance) % len(devices), i) for i in devices]
    return lax.ppermute(block, axis, route)


def dequantize(codes, exponents):
    points, columns = codes.shape
    blocks = exponents.shape[1]
    factor = jnp.zeros(exponents.shape, jnp.float32)
    for level_index in range(4):
        factor = factor + jnp.where(exponents == level_index, 2.0 ** (level_index - 9), 0.0)
    scaled_codes = (
        codes.reshape(points, blocks, columns // blocks).astype(jnp.float32) * factor[:, :, None]
    )
    return scaled_codes.reshape(points, columns).astype(jnp.bfloat16)


def squares(points_bf):
    widened = points_bf.astype(jnp.float32)
    return jnp.sum(widened * widened, axis=1)


def kernel_block(targets_bf, sources_bf, source_sq, rhs_values):
    target_sq = squares(targets_bf)
    inner_products = lax.dot_general(
        targets_bf, sources_bf, (((1,), (1,)), ((), ())), preferred_element_type=jnp.float32
    )
    squared = target_sq[:, None] + source_sq[None, :] - 2.0 * inner_products
    scaled = kernel_rate * jnp.sqrt(squared) / math.sqrt(targets_bf.shape[1])
    matern = ((1.0 + scaled + scaled * scaled / 3.0) * jnp.exp(-scaled)).astype(jnp.bfloat16)
    return lax.dot_general(
        rhs_values, matern, (((0,), (1,)), ((), ())), preferred_element_type=jnp.float32
    )


def halving_scatter(sums, axis):
    size = lax.axis_size(axis)
    me = lax.axis_index(axis)
    bits = size.bit_length() - 1
    rows, cols = sums.shape
    chunk = rows // size
    parts = sums.reshape((2,) * bits + (chunk, cols))
    order = [b for b in (0, 1, 3, 2) if b < bits] + [b for b in range(bits) if b not in (0, 1, 3, 2)]
    remaining = list(range(bits - 1, -1, -1))
    for bit in order:
        position = remaining.index(bit)
        mine = (me >> bit) & 1
        kept = lax.dynamic_index_in_dim(parts, mine, position, keepdims=False)
        sent = lax.dynamic_index_in_dim(parts, 1 - mine, position, keepdims=False)
        route = [(i, i ^ (1 << bit)) for i in range(size)]
        parts = kept + lax.ppermute(sent, axis, route)
        remaining.pop(position)
    return parts.reshape(chunk, cols)


def per_device(src_codes, src_exps, signs, tgt_codes, tgt_exps):
    sources_bf = dequantize(src_codes, src_exps)
    targets_bf = dequantize(tgt_codes, tgt_exps)
    rhs_values = (2 * signs - 1).astype(jnp.bfloat16)
    source_sq = squares(sources_bf)
    cycle_size = lax.axis_size("blk")
    group_size = lax.axis_size("grp")
    block_rows = targets_bf.shape[0]
    rhs_count = rhs_values.shape[1]

    def contribution(points_bf):
        return kernel_block(points_bf, sources_bf, source_sq, rhs_values)

    def advance(counter, carried):
        points_bf, running = carried
        running = running + contribution(points_bf)
        points_bf = shifted(points_bf, "blk", 1)
        running = shifted(running, "blk", 1)
        return (points_bf, running)

    start_sums = jnp.zeros((rhs_count, block_rows), jnp.float32)
    points_bf, running = lax.fori_loop(0, cycle_size - 1, advance, (targets_bf, start_sums))
    running = running + contribution(points_bf)
    gathered_sums = shifted(running, "blk", 1)
    owned_sums = halving_scatter(gathered_sums, "grp")
    source_total = src_codes.shape[0] * group_size * cycle_size
    return owned_sums.T * (4.0 / math.sqrt(source_total))


def solution(mesh):
    placed = (
        P(("grp", "blk"), None),
        P(("grp", "blk"), None),
        P(("grp", "blk"), None),
        P("blk", None),
        P("blk", None),
    )
    return jax.shard_map(
        per_device, mesh=mesh, in_specs=placed, out_specs=P("blk", "grp"), check_vma=False
    )
```

```python
import math

import jax
import jax.numpy as jnp
from jax import lax
from jax.sharding import PartitionSpec as P

kernel_rate = 20.0


def shifted(block, axis, distance):
    devices = range(lax.axis_size(axis))
    route = [((i - distance) % len(devices), i) for i in devices]
    return lax.ppermute(block, axis, route)


def dequantize(codes, exponents):
    points, columns = codes.shape
    blocks = exponents.shape[1]
    factor = jnp.zeros(exponents.shape, jnp.float32)
    for level_index in range(4):
        factor = factor + jnp.where(exponents == level_index, 2.0 ** (level_index - 9), 0.0)
    scaled_codes = (
        codes.reshape(points, blocks, columns // blocks).astype(jnp.float32) * factor[:, :, None]
    )
    return scaled_codes.reshape(points, columns).astype(jnp.bfloat16)


def squares(points_bf):
    widened = points_bf.astype(jnp.float32)
    return jnp.sum(widened * widened, axis=1)


def kernel_block(targets_bf, sources_bf, source_sq, rhs_values):
    target_sq = squares(targets_bf)
    inner_products = lax.dot_general(
        targets_bf, sources_bf, (((1,), (1,)), ((), ())), preferred_element_type=jnp.float32
    )
    squared = target_sq[:, None] + source_sq[None, :] - 2.0 * inner_products
    scaled = kernel_rate * jnp.sqrt(squared) / math.sqrt(targets_bf.shape[1])
    matern = ((1.0 + scaled + scaled * scaled / 3.0) * jnp.exp(-scaled)).astype(jnp.bfloat16)
    return lax.dot_general(
        rhs_values, matern, (((0,), (1,)), ((), ())), preferred_element_type=jnp.float32
    )


def halving_scatter(sums, axis):
    size = lax.axis_size(axis)
    me = lax.axis_index(axis)
    bits = size.bit_length() - 1
    rows, cols = sums.shape
    chunk = rows // size
    parts = sums.reshape((2,) * bits + (chunk, cols))
    order = [b for b in (0, 1, 3, 2) if b < bits] + [b for b in range(bits) if b not in (0, 1, 3, 2)]
    remaining = list(range(bits - 1, -1, -1))
    for bit in order:
        position = remaining.index(bit)
        mine = (me >> bit) & 1
        kept = lax.dynamic_index_in_dim(parts, mine, position, keepdims=False)
        sent = lax.dynamic_index_in_dim(parts, 1 - mine, position, keepdims=False)
        route = [(i, i ^ (1 << bit)) for i in range(size)]
        parts = kept + lax.ppermute(sent, axis, route)
        remaining.pop(position)
    return parts.reshape(chunk, cols)


def ring_order(size):
    if size == 16:
        chips = [(0, 0), (1, 0), (2, 0), (3, 0), (3, 1), (2, 1), (1, 1), (0, 1)]
        return [(x * 2 + y) * 2 + core for x, y in chips for core in (0, 1)]
    return list(range(size))


def per_device(src_codes, src_exps, signs, tgt_codes, tgt_exps):
    sources_bf = dequantize(src_codes, src_exps)
    targets_bf = dequantize(tgt_codes, tgt_exps)
    rhs_values = (2 * signs - 1).astype(jnp.bfloat16)
    source_sq = squares(sources_bf)
    cycle_size = lax.axis_size("blk")
    group_size = lax.axis_size("grp")
    block_rows = targets_bf.shape[0]
    half = block_rows // 2
    order = ring_order(cycle_size)
    forward = [(order[i], order[(i + 1) % cycle_size]) for i in range(cycle_size)]
    backward = [(b, a) for a, b in forward]

    def contribution(points_bf):
        return kernel_block(points_bf, sources_bf, source_sq, rhs_values)

    def step(points_f, points_b, sums_f, sums_b):
        both = contribution(jnp.concatenate([points_f, points_b], axis=0))
        sums_f = lax.ppermute(sums_f + both[:, :half], "blk", forward)
        sums_b = lax.ppermute(sums_b + both[:, half:], "blk", backward)
        return sums_f, sums_b

    def advance(counter, carried):
        points_f, points_b, sums_f, sums_b = carried
        next_f = lax.ppermute(points_f, "blk", forward)
        next_b = lax.ppermute(points_b, "blk", backward)
        sums_f, sums_b = step(points_f, points_b, sums_f, sums_b)
        return (next_f, next_b, sums_f, sums_b)

    points_f = lax.ppermute(targets_bf[:half], "blk", forward)
    points_b = lax.ppermute(targets_bf[half:], "blk", backward)
    own = contribution(targets_bf)
    rhs_count = rhs_values.shape[1]
    zeros = jnp.zeros((rhs_count, half), jnp.float32)
    carried = lax.fori_loop(0, cycle_size - 2, advance, (points_f, points_b, zeros, zeros))
    sums_f, sums_b = step(*carried)
    gathered_sums = own + jnp.concatenate([sums_f, sums_b], axis=1)
    owned_sums = halving_scatter(gathered_sums, "grp")
    source_total = src_codes.shape[0] * group_size * cycle_size
    return owned_sums.T * (4.0 / math.sqrt(source_total))


def solution(mesh):
    placed = (
        P(("grp", "blk"), None),
        P(("grp", "blk"), None),
        P(("grp", "blk"), None),
        P("blk", None),
        P("blk", None),
    )
    return jax.shard_map(
        per_device, mesh=mesh, in_specs=placed, out_specs=P("blk", "grp"), check_vma=False
    )
```

```python
import math

import jax
import jax.numpy as jnp
from jax import lax
from jax.sharding import PartitionSpec as P

kernel_rate = 20.0


def shifted(block, axis, distance):
    devices = range(lax.axis_size(axis))
    route = [((i - distance) % len(devices), i) for i in devices]
    return lax.ppermute(block, axis, route)


def dequantize(codes, exponents):
    points, columns = codes.shape
    blocks = exponents.shape[1]
    factor = jnp.zeros(exponents.shape, jnp.float32)
    for level_index in range(4):
        factor = factor + jnp.where(exponents == level_index, 2.0 ** (level_index - 9), 0.0)
    scaled_codes = (
        codes.reshape(points, blocks, columns // blocks).astype(jnp.float32) * factor[:, :, None]
    )
    return scaled_codes.reshape(points, columns).astype(jnp.bfloat16)


def squares(points_bf):
    widened = points_bf.astype(jnp.float32)
    return jnp.sum(widened * widened, axis=1)


def kernel_block(targets_bf, sources_bf, source_sq, rhs_values):
    target_sq = squares(targets_bf)
    inner_products = lax.dot_general(
        targets_bf, sources_bf, (((1,), (1,)), ((), ())), preferred_element_type=jnp.float32
    )
    squared = target_sq[:, None] + source_sq[None, :] - 2.0 * inner_products
    scaled = kernel_rate * jnp.sqrt(squared) / math.sqrt(targets_bf.shape[1])
    matern = ((1.0 + scaled + scaled * scaled / 3.0) * jnp.exp(-scaled)).astype(jnp.bfloat16)
    return lax.dot_general(
        rhs_values, matern, (((0,), (1,)), ((), ())), preferred_element_type=jnp.float32
    )


def halving_scatter(sums, axis):
    size = lax.axis_size(axis)
    me = lax.axis_index(axis)
    bits = size.bit_length() - 1
    rows, cols = sums.shape
    chunk = rows // size
    parts = sums.reshape((2,) * bits + (chunk, cols))
    order = [b for b in (0, 1, 3, 2) if b < bits] + [b for b in range(bits) if b not in (0, 1, 3, 2)]
    remaining = list(range(bits - 1, -1, -1))
    for bit in order:
        position = remaining.index(bit)
        mine = (me >> bit) & 1
        kept = lax.dynamic_index_in_dim(parts, mine, position, keepdims=False)
        sent = lax.dynamic_index_in_dim(parts, 1 - mine, position, keepdims=False)
        route = [(i, i ^ (1 << bit)) for i in range(size)]
        parts = kept + lax.ppermute(sent, axis, route)
        remaining.pop(position)
    return parts.reshape(chunk, cols)


def ring_order(size):
    if size == 16:
        chips = [(0, 0), (1, 0), (2, 0), (3, 0), (3, 1), (2, 1), (1, 1), (0, 1)]
        return [(x * 2 + y) * 2 + core for x, y in chips for core in (0, 1)]
    return list(range(size))


def per_device(src_codes, src_exps, signs, tgt_codes, tgt_exps):
    sources_bf = dequantize(src_codes, src_exps)
    targets_bf = dequantize(tgt_codes, tgt_exps)
    rhs_values = (2 * signs - 1).astype(jnp.bfloat16)
    source_sq = squares(sources_bf)
    cycle_size = lax.axis_size("blk")
    group_size = lax.axis_size("grp")
    block_rows = targets_bf.shape[0]
    half = block_rows // 2
    order = ring_order(cycle_size)
    forward = [(order[i], order[(i + 1) % cycle_size]) for i in range(cycle_size)]
    backward = [(b, a) for a, b in forward]

    def contribution(points_bf):
        return kernel_block(points_bf, sources_bf, source_sq, rhs_values)

    def halves(points_f, points_b):
        both = contribution(jnp.concatenate([points_f, points_b], axis=0))
        return both[:, :half], both[:, half:]

    def send(points_f, points_b):
        return lax.ppermute(points_f, "blk", forward), lax.ppermute(points_b, "blk", backward)

    def advance(counter, carried):
        points_f, points_b, sums_f, sums_b, part_f, part_b = carried
        sums_f, sums_b = send(sums_f + part_f, sums_b + part_b)
        next_f, next_b = send(points_f, points_b)
        part_f, part_b = halves(points_f, points_b)
        return (next_f, next_b, sums_f, sums_b, part_f, part_b)

    points_f, points_b = send(targets_bf[:half], targets_bf[half:])
    own = contribution(targets_bf)
    next_f, next_b = send(points_f, points_b)
    part_f, part_b = halves(points_f, points_b)
    zeros = jnp.zeros_like(part_f)
    carried = (next_f, next_b, zeros, zeros, part_f, part_b)
    carried = lax.fori_loop(0, cycle_size - 3, advance, carried)
    points_f, points_b, sums_f, sums_b, part_f, part_b = carried
    sums_f, sums_b = send(sums_f + part_f, sums_b + part_b)
    part_f, part_b = halves(points_f, points_b)
    sums_f, sums_b = send(sums_f + part_f, sums_b + part_b)
    gathered_sums = own + jnp.concatenate([sums_f, sums_b], axis=1)
    owned_sums = halving_scatter(gathered_sums, "grp")
    source_total = src_codes.shape[0] * group_size * cycle_size
    return owned_sums.T * (4.0 / math.sqrt(source_total))


def solution(mesh):
    placed = (
        P(("grp", "blk"), None),
        P(("grp", "blk"), None),
        P(("grp", "blk"), None),
        P("blk", None),
        P("blk", None),
    )
    return jax.shard_map(
        per_device, mesh=mesh, in_specs=placed, out_specs=P("blk", "grp"), check_vma=False
    )
```

```python
import math

import jax
import jax.numpy as jnp
from jax import lax
from jax.sharding import PartitionSpec as P

kernel_rate = 20.0


def shifted(block, axis, distance):
    devices = range(lax.axis_size(axis))
    route = [((i - distance) % len(devices), i) for i in devices]
    return lax.ppermute(block, axis, route)


def dequantize(codes, exponents):
    points, columns = codes.shape
    blocks = exponents.shape[1]
    factor = jnp.zeros(exponents.shape, jnp.float32)
    for level_index in range(4):
        factor = factor + jnp.where(exponents == level_index, 2.0 ** (level_index - 9), 0.0)
    scaled_codes = (
        codes.reshape(points, blocks, columns // blocks).astype(jnp.float32) * factor[:, :, None]
    )
    return scaled_codes.reshape(points, columns).astype(jnp.bfloat16)


def squares(points_bf):
    widened = points_bf.astype(jnp.float32)
    return jnp.sum(widened * widened, axis=1)


def kernel_block(targets_bf, sources_bf, source_sq, rhs_values):
    target_sq = squares(targets_bf)
    inner_products = lax.dot_general(
        targets_bf, sources_bf, (((1,), (1,)), ((), ())), preferred_element_type=jnp.float32
    )
    squared = target_sq[:, None] + source_sq[None, :] - 2.0 * inner_products
    scaled = kernel_rate * jnp.sqrt(squared) / math.sqrt(targets_bf.shape[1])
    matern = ((1.0 + scaled + scaled * scaled / 3.0) * jnp.exp(-scaled)).astype(jnp.bfloat16)
    return lax.dot_general(
        rhs_values, matern, (((0,), (1,)), ((), ())), preferred_element_type=jnp.float32
    )


def halving_scatter(sums, axis):
    size = lax.axis_size(axis)
    me = lax.axis_index(axis)
    bits = size.bit_length() - 1
    rows, cols = sums.shape
    chunk = rows // size
    parts = sums.reshape((2,) * bits + (chunk, cols))
    order = [b for b in (0, 1, 3, 2) if b < bits] + [b for b in range(bits) if b not in (0, 1, 3, 2)]
    remaining = list(range(bits - 1, -1, -1))
    for bit in order:
        position = remaining.index(bit)
        mine = (me >> bit) & 1
        kept = lax.dynamic_index_in_dim(parts, mine, position, keepdims=False)
        sent = lax.dynamic_index_in_dim(parts, 1 - mine, position, keepdims=False)
        route = [(i, i ^ (1 << bit)) for i in range(size)]
        parts = kept + lax.ppermute(sent, axis, route)
        remaining.pop(position)
    return parts.reshape(chunk, cols)


def ring_order(size):
    if size == 16:
        chips = [(0, 0), (1, 0), (2, 0), (3, 0), (3, 1), (2, 1), (1, 1), (0, 1)]
        return [(x * 2 + y) * 2 + core for x, y in chips for core in (0, 1)]
    return list(range(size))


def per_device(src_codes, src_exps, signs, tgt_codes, tgt_exps):
    sources_bf = dequantize(src_codes, src_exps)
    targets_bf = dequantize(tgt_codes, tgt_exps)
    rhs_values = (2 * signs - 1).astype(jnp.bfloat16)
    source_sq = squares(sources_bf)
    cycle_size = lax.axis_size("blk")
    group_size = lax.axis_size("grp")
    block_rows = targets_bf.shape[0]
    half = block_rows // 2
    order = ring_order(cycle_size)
    forward = [(order[i], order[(i + 1) % cycle_size]) for i in range(cycle_size)]
    backward = [(b, a) for a, b in forward]

    def contribution(points_bf):
        return kernel_block(points_bf, sources_bf, source_sq, rhs_values)

    def halves(points_f, points_b):
        both = contribution(jnp.concatenate([points_f, points_b], axis=0))
        return both[:, :half], both[:, half:]

    def send(points_f, points_b):
        return lax.ppermute(points_f, "blk", forward), lax.ppermute(points_b, "blk", backward)

    width = targets_bf.shape[1]
    rhs_count = rhs_values.shape[1]
    sum_shape = (rhs_count, half)
    sum_rows = rhs_count * half // width

    def pack(points, sums):
        high = lax.reduce_precision(sums, exponent_bits=8, mantissa_bits=7)
        low = (sums - high).astype(jnp.bfloat16)
        parts = [points, high.astype(jnp.bfloat16).reshape(-1, width), low.reshape(-1, width)]
        return jnp.concatenate(parts, axis=0)

    def unpack(packed):
        points = packed[:half]
        high = packed[half : half + sum_rows].reshape(sum_shape).astype(jnp.float32)
        low = packed[half + sum_rows :].reshape(sum_shape).astype(jnp.float32)
        return points, high + low

    def advance(counter, carried):
        packed_f, packed_b, part_f, part_b = carried
        points_f, sums_f = unpack(packed_f)
        points_b, sums_b = unpack(packed_b)
        packed_f, packed_b = send(pack(points_f, sums_f + part_f), pack(points_b, sums_b + part_b))
        part_f, part_b = halves(points_f, points_b)
        return (packed_f, packed_b, part_f, part_b)

    zeros = jnp.zeros(sum_shape, jnp.float32)
    packed_f, packed_b = send(pack(targets_bf[:half], zeros), pack(targets_bf[half:], zeros))
    own = contribution(targets_bf)
    carried = lax.fori_loop(0, cycle_size - 1, advance, (packed_f, packed_b, zeros, zeros))
    packed_f, packed_b, part_f, part_b = carried
    sums_f = unpack(packed_f)[1] + part_f
    sums_b = unpack(packed_b)[1] + part_b
    sums_f, sums_b = send(sums_f, sums_b)
    gathered_sums = own + jnp.concatenate([sums_f, sums_b], axis=1)
    owned_sums = halving_scatter(gathered_sums, "grp")
    source_total = src_codes.shape[0] * group_size * cycle_size
    return owned_sums.T * (4.0 / math.sqrt(source_total))


def solution(mesh):
    placed = (
        P(("grp", "blk"), None),
        P(("grp", "blk"), None),
        P(("grp", "blk"), None),
        P("blk", None),
        P("blk", None),
    )
    return jax.shard_map(
        per_device, mesh=mesh, in_specs=placed, out_specs=P("blk", "grp"), check_vma=False
    )
```

```python
import math

import jax
import jax.numpy as jnp
from jax import lax
from jax.sharding import PartitionSpec as P

kernel_rate = 20.0


def shifted(block, axis, distance):
    devices = range(lax.axis_size(axis))
    route = [((i - distance) % len(devices), i) for i in devices]
    return lax.ppermute(block, axis, route)


def dequantize(codes, exponents):
    points, columns = codes.shape
    blocks = exponents.shape[1]
    factor = jnp.zeros(exponents.shape, jnp.float32)
    for level_index in range(4):
        factor = factor + jnp.where(exponents == level_index, 2.0 ** (level_index - 9), 0.0)
    scaled_codes = (
        codes.reshape(points, blocks, columns // blocks).astype(jnp.float32) * factor[:, :, None]
    )
    return scaled_codes.reshape(points, columns).astype(jnp.bfloat16)


def squares(points_bf):
    widened = points_bf.astype(jnp.float32)
    return jnp.sum(widened * widened, axis=1)


def kernel_block(targets_bf, sources_bf, source_sq, rhs_values):
    target_sq = squares(targets_bf)
    inner_products = lax.dot_general(
        targets_bf, sources_bf, (((1,), (1,)), ((), ())), preferred_element_type=jnp.float32
    )
    squared = target_sq[:, None] + source_sq[None, :] - 2.0 * inner_products
    scaled = kernel_rate * jnp.sqrt(squared) / math.sqrt(targets_bf.shape[1])
    matern = ((1.0 + scaled + scaled * scaled / 3.0) * jnp.exp(-scaled)).astype(jnp.bfloat16)
    return lax.dot_general(
        rhs_values, matern, (((0,), (1,)), ((), ())), preferred_element_type=jnp.float32
    )


def exchange_scatter(sums, axis):
    size = lax.axis_size(axis)
    rows, cols = sums.shape
    pieces = sums.reshape(size, rows // size, cols)
    pieces = lax.all_to_all(pieces, axis, 0, 0, tiled=False)
    return jnp.sum(pieces, axis=0)


def halving_scatter(sums, axis):
    size = lax.axis_size(axis)
    me = lax.axis_index(axis)
    bits = size.bit_length() - 1
    rows, cols = sums.shape
    chunk = rows // size
    parts = sums.reshape((2,) * bits + (chunk, cols))
    order = [b for b in (0, 1, 3, 2) if b < bits] + [b for b in range(bits) if b not in (0, 1, 3, 2)]
    remaining = list(range(bits - 1, -1, -1))
    for bit in order:
        position = remaining.index(bit)
        mine = (me >> bit) & 1
        kept = lax.dynamic_index_in_dim(parts, mine, position, keepdims=False)
        sent = lax.dynamic_index_in_dim(parts, 1 - mine, position, keepdims=False)
        route = [(i, i ^ (1 << bit)) for i in range(size)]
        parts = kept + lax.ppermute(sent, axis, route)
        remaining.pop(position)
    return parts.reshape(chunk, cols)


def ring_order(size):
    if size == 16:
        chips = [(0, 0), (1, 0), (2, 0), (3, 0), (3, 1), (2, 1), (1, 1), (0, 1)]
        return [(x * 2 + y) * 2 + core for x, y in chips for core in (0, 1)]
    return list(range(size))


def per_device(src_codes, src_exps, signs, tgt_codes, tgt_exps):
    sources_bf = dequantize(src_codes, src_exps)
    targets_bf = dequantize(tgt_codes, tgt_exps)
    rhs_values = (2 * signs - 1).astype(jnp.bfloat16)
    source_sq = squares(sources_bf)
    cycle_size = lax.axis_size("blk")
    group_size = lax.axis_size("grp")
    block_rows = targets_bf.shape[0]
    half = block_rows // 2
    order = ring_order(cycle_size)
    forward = [(order[i], order[(i + 1) % cycle_size]) for i in range(cycle_size)]
    backward = [(b, a) for a, b in forward]

    def contribution(points_bf):
        return kernel_block(points_bf, sources_bf, source_sq, rhs_values)

    def halves(points_f, points_b):
        both = contribution(jnp.concatenate([points_f, points_b], axis=0))
        return both[:, :half], both[:, half:]

    def send(points_f, points_b):
        return lax.ppermute(points_f, "blk", forward), lax.ppermute(points_b, "blk", backward)

    def advance(counter, carried):
        points_f, points_b, sums_f, sums_b, part_f, part_b = carried
        sums_f, sums_b = send(sums_f + part_f, sums_b + part_b)
        next_f, next_b = send(points_f, points_b)
        part_f, part_b = halves(points_f, points_b)
        return (next_f, next_b, sums_f, sums_b, part_f, part_b)

    points_f, points_b = send(targets_bf[:half], targets_bf[half:])
    own = contribution(targets_bf)
    next_f, next_b = send(points_f, points_b)
    part_f, part_b = halves(points_f, points_b)
    zeros = jnp.zeros_like(part_f)
    carried = (next_f, next_b, zeros, zeros, part_f, part_b)
    carried = lax.fori_loop(0, cycle_size - 3, advance, carried)
    points_f, points_b, sums_f, sums_b, part_f, part_b = carried
    sums_f, sums_b = send(sums_f + part_f, sums_b + part_b)
    part_f, part_b = halves(points_f, points_b)
    sums_f, sums_b = send(sums_f + part_f, sums_b + part_b)
    gathered_sums = own + jnp.concatenate([sums_f, sums_b], axis=1)
    owned_sums = exchange_scatter(gathered_sums, "grp")
    source_total = src_codes.shape[0] * group_size * cycle_size
    return owned_sums.T * (4.0 / math.sqrt(source_total))


def solution(mesh):
    placed = (
        P(("grp", "blk"), None),
        P(("grp", "blk"), None),
        P(("grp", "blk"), None),
        P("blk", None),
        P("blk", None),
    )
    return jax.shard_map(
        per_device, mesh=mesh, in_specs=placed, out_specs=P("blk", "grp"), check_vma=False
    )
```

```python
import math

import jax
import jax.numpy as jnp
from jax import lax
from jax.sharding import PartitionSpec as P

kernel_rate = 20.0


def shifted(block, axis, distance):
    devices = range(lax.axis_size(axis))
    route = [((i - distance) % len(devices), i) for i in devices]
    return lax.ppermute(block, axis, route)


def dequantize(codes, exponents):
    points, columns = codes.shape
    blocks = exponents.shape[1]
    factor = jnp.zeros(exponents.shape, jnp.float32)
    for level_index in range(4):
        factor = factor + jnp.where(exponents == level_index, 2.0 ** (level_index - 9), 0.0)
    scaled_codes = (
        codes.reshape(points, blocks, columns // blocks).astype(jnp.float32) * factor[:, :, None]
    )
    return scaled_codes.reshape(points, columns).astype(jnp.bfloat16)


def squares(points_bf):
    widened = points_bf.astype(jnp.float32)
    return jnp.sum(widened * widened, axis=1)


def kernel_block(targets_bf, sources_bf, source_sq, rhs_values):
    target_sq = squares(targets_bf)
    inner_products = lax.dot_general(
        targets_bf, sources_bf, (((1,), (1,)), ((), ())), preferred_element_type=jnp.float32
    )
    squared = target_sq[:, None] + source_sq[None, :] - 2.0 * inner_products
    scaled = kernel_rate * jnp.sqrt(squared) / math.sqrt(targets_bf.shape[1])
    matern = ((1.0 + scaled + scaled * scaled / 3.0) * jnp.exp(-scaled)).astype(jnp.bfloat16)
    return lax.dot_general(
        rhs_values, matern, (((0,), (1,)), ((), ())), preferred_element_type=jnp.float32
    )


def radix_scatter(sums, axis, groups=((0, 1), (2, 3))):
    size = lax.axis_size(axis)
    me = lax.axis_index(axis)
    bits = size.bit_length() - 1
    if size != 16:
        return halving_scatter(sums, axis)
    rows, cols = sums.shape
    chunk = rows // size
    parts = sums.reshape((2,) * bits + (chunk, cols))
    remaining = list(range(bits - 1, -1, -1))

    def select(values, group):
        picked = parts
        for bit in sorted(group, key=remaining.index, reverse=True):
            picked = lax.dynamic_index_in_dim(picked, values[bit], remaining.index(bit), keepdims=False)
        return picked

    for group in groups:
        mine = {bit: (me >> bit) & 1 for bit in group}
        total = select(mine, group)
        for code in range(1, 1 << len(group)):
            offset = sum(((code >> k) & 1) << bit for k, bit in enumerate(group))
            theirs = {bit: mine[bit] ^ ((offset >> bit) & 1) for bit in group}
            route = [(i, i ^ offset) for i in range(size)]
            total = total + lax.ppermute(select(theirs, group), axis, route)
        parts = total
        for bit in group:
            remaining.remove(bit)
    return parts.reshape(chunk, cols)


def halving_scatter(sums, axis):
    size = lax.axis_size(axis)
    me = lax.axis_index(axis)
    bits = size.bit_length() - 1
    rows, cols = sums.shape
    chunk = rows // size
    parts = sums.reshape((2,) * bits + (chunk, cols))
    order = [b for b in (0, 1, 3, 2) if b < bits] + [b for b in range(bits) if b not in (0, 1, 3, 2)]
    remaining = list(range(bits - 1, -1, -1))
    for bit in order:
        position = remaining.index(bit)
        mine = (me >> bit) & 1
        kept = lax.dynamic_index_in_dim(parts, mine, position, keepdims=False)
        sent = lax.dynamic_index_in_dim(parts, 1 - mine, position, keepdims=False)
        route = [(i, i ^ (1 << bit)) for i in range(size)]
        parts = kept + lax.ppermute(sent, axis, route)
        remaining.pop(position)
    return parts.reshape(chunk, cols)


def ring_order(size):
    if size == 16:
        chips = [(0, 0), (1, 0), (2, 0), (3, 0), (3, 1), (2, 1), (1, 1), (0, 1)]
        return [(x * 2 + y) * 2 + core for x, y in chips for core in (0, 1)]
    return list(range(size))


def per_device(src_codes, src_exps, signs, tgt_codes, tgt_exps):
    sources_bf = dequantize(src_codes, src_exps)
    targets_bf = dequantize(tgt_codes, tgt_exps)
    rhs_values = (2 * signs - 1).astype(jnp.bfloat16)
    source_sq = squares(sources_bf)
    cycle_size = lax.axis_size("blk")
    group_size = lax.axis_size("grp")
    block_rows = targets_bf.shape[0]
    half = block_rows // 2
    order = ring_order(cycle_size)
    forward = [(order[i], order[(i + 1) % cycle_size]) for i in range(cycle_size)]
    backward = [(b, a) for a, b in forward]

    def contribution(points_bf):
        return kernel_block(points_bf, sources_bf, source_sq, rhs_values)

    def halves(points_f, points_b):
        both = contribution(jnp.concatenate([points_f, points_b], axis=0))
        return both[:, :half], both[:, half:]

    def send(points_f, points_b):
        return lax.ppermute(points_f, "blk", forward), lax.ppermute(points_b, "blk", backward)

    def advance(counter, carried):
        points_f, points_b, sums_f, sums_b, part_f, part_b = carried
        sums_f, sums_b = send(sums_f + part_f, sums_b + part_b)
        next_f, next_b = send(points_f, points_b)
        part_f, part_b = halves(points_f, points_b)
        return (next_f, next_b, sums_f, sums_b, part_f, part_b)

    points_f, points_b = send(targets_bf[:half], targets_bf[half:])
    own = lax.optimization_barrier(contribution(targets_bf))
    next_f, next_b = send(points_f, points_b)
    part_f, part_b = halves(points_f, points_b)
    zeros = jnp.zeros_like(part_f)
    carried = (next_f, next_b, zeros, zeros, part_f, part_b)
    carried = lax.fori_loop(0, cycle_size - 3, advance, carried)
    points_f, points_b, sums_f, sums_b, part_f, part_b = carried
    sums_f, sums_b = send(sums_f + part_f, sums_b + part_b)
    part_f, part_b = halves(points_f, points_b)
    sums_f, sums_b = send(sums_f + part_f, sums_b + part_b)
    gathered_sums = own + jnp.concatenate([sums_f, sums_b], axis=1)
    owned_sums = radix_scatter(gathered_sums, "grp")
    source_total = src_codes.shape[0] * group_size * cycle_size
    return owned_sums.T * (4.0 / math.sqrt(source_total))


def solution(mesh):
    placed = (
        P(("grp", "blk"), None),
        P(("grp", "blk"), None),
        P(("grp", "blk"), None),
        P("blk", None),
        P("blk", None),
    )
    return jax.shard_map(
        per_device, mesh=mesh, in_specs=placed, out_specs=P("blk", "grp"), check_vma=False
    )
```

```python
import math

import jax
import jax.numpy as jnp
from jax import lax
from jax.sharding import PartitionSpec as P

kernel_rate = 20.0


def shifted(block, axis, distance):
    devices = range(lax.axis_size(axis))
    route = [((i - distance) % len(devices), i) for i in devices]
    return lax.ppermute(block, axis, route)


def dequantize(codes, exponents):
    points, columns = codes.shape
    blocks = exponents.shape[1]
    factor = jnp.zeros(exponents.shape, jnp.float32)
    for level_index in range(4):
        factor = factor + jnp.where(exponents == level_index, 2.0 ** (level_index - 9), 0.0)
    scaled_codes = (
        codes.reshape(points, blocks, columns // blocks).astype(jnp.float32) * factor[:, :, None]
    )
    return scaled_codes.reshape(points, columns).astype(jnp.bfloat16)


def squares(points_bf):
    widened = points_bf.astype(jnp.float32)
    return jnp.sum(widened * widened, axis=1)


def kernel_block(targets_bf, sources_bf, source_sq, rhs_values):
    target_sq = squares(targets_bf)
    inner_products = lax.dot_general(
        targets_bf, sources_bf, (((1,), (1,)), ((), ())), preferred_element_type=jnp.float32
    )
    squared = target_sq[:, None] + source_sq[None, :] - 2.0 * inner_products
    scaled = kernel_rate * jnp.sqrt(squared) / math.sqrt(targets_bf.shape[1])
    matern = ((1.0 + scaled + scaled * scaled / 3.0) * jnp.exp(-scaled)).astype(jnp.bfloat16)
    return lax.dot_general(
        rhs_values, matern, (((0,), (1,)), ((), ())), preferred_element_type=jnp.float32
    )


def halving_scatter(sums, axis):
    size = lax.axis_size(axis)
    me = lax.axis_index(axis)
    bits = size.bit_length() - 1
    rows, cols = sums.shape
    chunk = rows // size
    parts = sums.reshape((2,) * bits + (chunk, cols))
    order = [b for b in (0, 1, 3, 2) if b < bits] + [b for b in range(bits) if b not in (0, 1, 3, 2)]
    remaining = list(range(bits - 1, -1, -1))
    for bit in order:
        position = remaining.index(bit)
        mine = (me >> bit) & 1
        kept = lax.dynamic_index_in_dim(parts, mine, position, keepdims=False)
        sent = lax.dynamic_index_in_dim(parts, 1 - mine, position, keepdims=False)
        route = [(i, i ^ (1 << bit)) for i in range(size)]
        parts = kept + lax.ppermute(sent, axis, route)
        remaining.pop(position)
    return parts.reshape(chunk, cols)


def ring_order(size):
    if size == 16:
        chips = [(0, 0), (1, 0), (2, 0), (3, 0), (3, 1), (2, 1), (1, 1), (0, 1)]
        return [(x * 2 + y) * 2 + core for x, y in chips for core in (0, 1)]
    return list(range(size))


def per_device(src_codes, src_exps, signs, tgt_codes, tgt_exps):
    sources_bf = dequantize(src_codes, src_exps)
    targets_bf = dequantize(tgt_codes, tgt_exps)
    rhs_values = (2 * signs - 1).astype(jnp.bfloat16)
    source_sq = squares(sources_bf)
    cycle_size = lax.axis_size("blk")
    group_size = lax.axis_size("grp")
    block_rows = targets_bf.shape[0]
    half = block_rows // 2
    order = ring_order(cycle_size)
    forward = [(order[i], order[(i + 1) % cycle_size]) for i in range(cycle_size)]
    backward = [(b, a) for a, b in forward]

    def contribution(points_bf):
        return kernel_block(points_bf, sources_bf, source_sq, rhs_values)

    def halves(points_f, points_b):
        both = contribution(jnp.concatenate([points_f, points_b], axis=0))
        return both[:, :half], both[:, half:]

    def send(points_f, points_b):
        return lax.ppermute(points_f, "blk", forward), lax.ppermute(points_b, "blk", backward)

    def advance(counter, carried):
        points_f, points_b, sums_f, sums_b, part_f, part_b = carried
        sums_f, sums_b = send(sums_f + part_f, sums_b + part_b)
        next_f, next_b = send(points_f, points_b)
        part_f, part_b = halves(points_f, points_b)
        return (next_f, next_b, sums_f, sums_b, part_f, part_b)

    points_f, points_b = send(targets_bf[:half], targets_bf[half:])
    own = lax.optimization_barrier(contribution(targets_bf))
    next_f, next_b = send(points_f, points_b)
    part_f, part_b = halves(points_f, points_b)
    zeros = jnp.zeros_like(part_f)
    carried = (next_f, next_b, zeros, zeros, part_f, part_b)
    carried = lax.fori_loop(0, cycle_size - 3, advance, carried)
    points_f, points_b, sums_f, sums_b, part_f, part_b = carried
    sums_f, sums_b = send(sums_f + part_f, sums_b + part_b)
    part_f, part_b = halves(points_f, points_b)
    sums_f, sums_b = send(sums_f + part_f, sums_b + part_b)
    gathered_sums = own + jnp.concatenate([sums_f, sums_b], axis=1)
    owned_sums = halving_scatter(gathered_sums, "grp")
    source_total = src_codes.shape[0] * group_size * cycle_size
    return owned_sums.T * (4.0 / math.sqrt(source_total))


def solution(mesh):
    placed = (
        P(("grp", "blk"), None),
        P(("grp", "blk"), None),
        P(("grp", "blk"), None),
        P("blk", None),
        P("blk", None),
    )
    return jax.shard_map(
        per_device, mesh=mesh, in_specs=placed, out_specs=P("blk", "grp"), check_vma=False
    )
```

```python
import math

import jax
import jax.numpy as jnp
from jax import lax
from jax.sharding import PartitionSpec as P

kernel_rate = 20.0


def shifted(block, axis, distance):
    devices = range(lax.axis_size(axis))
    route = [((i - distance) % len(devices), i) for i in devices]
    return lax.ppermute(block, axis, route)


def dequantize(codes, exponents):
    points, columns = codes.shape
    blocks = exponents.shape[1]
    factor = jnp.zeros(exponents.shape, jnp.float32)
    for level_index in range(4):
        factor = factor + jnp.where(exponents == level_index, 2.0 ** (level_index - 9), 0.0)
    scaled_codes = (
        codes.reshape(points, blocks, columns // blocks).astype(jnp.float32) * factor[:, :, None]
    )
    return scaled_codes.reshape(points, columns).astype(jnp.bfloat16)


def squares(points_bf):
    widened = points_bf.astype(jnp.float32)
    return jnp.sum(widened * widened, axis=1)


def kernel_block(targets_bf, sources_bf, source_sq, rhs_values):
    target_sq = squares(targets_bf)
    inner_products = lax.dot_general(
        targets_bf, sources_bf, (((1,), (1,)), ((), ())), preferred_element_type=jnp.float32
    )
    squared = target_sq[:, None] + source_sq[None, :] - 2.0 * inner_products
    scaled = kernel_rate * jnp.sqrt(squared) / math.sqrt(targets_bf.shape[1])
    matern = ((1.0 + scaled + scaled * scaled / 3.0) * jnp.exp(-scaled)).astype(jnp.bfloat16)
    return lax.dot_general(
        rhs_values, matern, (((0,), (1,)), ((), ())), preferred_element_type=jnp.float32
    )


def halving_scatter(sums, axis):
    size = lax.axis_size(axis)
    me = lax.axis_index(axis)
    bits = size.bit_length() - 1
    rows, cols = sums.shape
    chunk = rows // size
    parts = sums.reshape((2,) * bits + (chunk, cols))
    order = [b for b in (0, 1, 3, 2) if b < bits] + [b for b in range(bits) if b not in (0, 1, 3, 2)]
    remaining = list(range(bits - 1, -1, -1))
    for bit in order:
        position = remaining.index(bit)
        mine = (me >> bit) & 1
        kept = lax.dynamic_index_in_dim(parts, mine, position, keepdims=False)
        sent = lax.dynamic_index_in_dim(parts, 1 - mine, position, keepdims=False)
        route = [(i, i ^ (1 << bit)) for i in range(size)]
        parts = kept + lax.ppermute(sent, axis, route)
        remaining.pop(position)
    return parts.reshape(chunk, cols)


def ring_order(size):
    if size == 16:
        chips = [(0, 0), (1, 0), (2, 0), (3, 0), (3, 1), (2, 1), (1, 1), (0, 1)]
        return [(x * 2 + y) * 2 + core for x, y in chips for core in (0, 1)]
    return list(range(size))


def per_device(src_codes, src_exps, signs, tgt_codes, tgt_exps):
    sources_bf = dequantize(src_codes, src_exps)
    targets_bf = dequantize(tgt_codes, tgt_exps)
    rhs_values = (2 * signs - 1).astype(jnp.bfloat16)
    source_sq = squares(sources_bf)
    cycle_size = lax.axis_size("blk")
    group_size = lax.axis_size("grp")
    block_rows = targets_bf.shape[0]
    half = block_rows // 2
    order = ring_order(cycle_size)
    forward = [(order[i], order[(i + 1) % cycle_size]) for i in range(cycle_size)]
    backward = [(b, a) for a, b in forward]

    def contribution(points_bf):
        return kernel_block(points_bf, sources_bf, source_sq, rhs_values)

    points_f = lax.ppermute(targets_bf[:half], "blk", forward)
    points_b = lax.ppermute(targets_bf[half:], "blk", backward)
    own = contribution(targets_bf)
    sums_f = sums_b = None
    for hop in range(1, cycle_size):
        if hop < cycle_size - 1:
            next_f = lax.ppermute(points_f, "blk", forward)
            next_b = lax.ppermute(points_b, "blk", backward)
        both = contribution(jnp.concatenate([points_f, points_b], axis=0))
        part_f, part_b = both[:, :half], both[:, half:]
        if sums_f is not None:
            part_f, part_b = sums_f + part_f, sums_b + part_b
        sums_f = lax.ppermute(part_f, "blk", forward)
        sums_b = lax.ppermute(part_b, "blk", backward)
        if hop < cycle_size - 1:
            points_f, points_b = next_f, next_b
    gathered_sums = own + jnp.concatenate([sums_f, sums_b], axis=1)
    owned_sums = halving_scatter(gathered_sums, "grp")
    source_total = src_codes.shape[0] * group_size * cycle_size
    return owned_sums.T * (4.0 / math.sqrt(source_total))


def solution(mesh):
    placed = (
        P(("grp", "blk"), None),
        P(("grp", "blk"), None),
        P(("grp", "blk"), None),
        P("blk", None),
        P("blk", None),
    )
    return jax.shard_map(
        per_device, mesh=mesh, in_specs=placed, out_specs=P("blk", "grp"), check_vma=False
    )
```

```python
import math

import jax
import jax.numpy as jnp
from jax import lax
from jax.sharding import PartitionSpec as P

kernel_rate = 20.0


def shifted(block, axis, distance):
    devices = range(lax.axis_size(axis))
    route = [((i - distance) % len(devices), i) for i in devices]
    return lax.ppermute(block, axis, route)


def dequantize(codes, exponents):
    points, columns = codes.shape
    blocks = exponents.shape[1]
    factor = jnp.zeros(exponents.shape, jnp.float32)
    for level_index in range(4):
        factor = factor + jnp.where(exponents == level_index, 2.0 ** (level_index - 9), 0.0)
    scaled_codes = (
        codes.reshape(points, blocks, columns // blocks).astype(jnp.float32) * factor[:, :, None]
    )
    return scaled_codes.reshape(points, columns).astype(jnp.bfloat16)


def squares(points_bf):
    widened = points_bf.astype(jnp.float32)
    return jnp.sum(widened * widened, axis=1)


def kernel_block(targets_bf, sources_bf, source_sq, rhs_values):
    target_sq = squares(targets_bf)
    inner_products = lax.dot_general(
        targets_bf, sources_bf, (((1,), (1,)), ((), ())), preferred_element_type=jnp.float32
    )
    squared = target_sq[:, None] + source_sq[None, :] - 2.0 * inner_products
    scaled = kernel_rate * jnp.sqrt(squared) / math.sqrt(targets_bf.shape[1])
    matern = ((1.0 + scaled + scaled * scaled / 3.0) * jnp.exp(-scaled)).astype(jnp.bfloat16)
    return lax.dot_general(
        rhs_values, matern, (((0,), (1,)), ((), ())), preferred_element_type=jnp.float32
    )


def exchange_scatter(sums, axis):
    size = lax.axis_size(axis)
    rows, cols = sums.shape
    pieces = sums.reshape(size, rows // size, cols)
    pieces = lax.all_to_all(pieces, axis, 0, 0, tiled=False)
    return jnp.sum(pieces, axis=0)


def halving_scatter(sums, axis):
    size = lax.axis_size(axis)
    me = lax.axis_index(axis)
    bits = size.bit_length() - 1
    rows, cols = sums.shape
    chunk = rows // size
    parts = sums.reshape((2,) * bits + (chunk, cols))
    order = [b for b in (0, 1, 3, 2) if b < bits] + [b for b in range(bits) if b not in (0, 1, 3, 2)]
    remaining = list(range(bits - 1, -1, -1))
    for bit in order:
        position = remaining.index(bit)
        mine = (me >> bit) & 1
        kept = lax.dynamic_index_in_dim(parts, mine, position, keepdims=False)
        sent = lax.dynamic_index_in_dim(parts, 1 - mine, position, keepdims=False)
        route = [(i, i ^ (1 << bit)) for i in range(size)]
        parts = kept + lax.ppermute(sent, axis, route)
        remaining.pop(position)
    return parts.reshape(chunk, cols)


def ring_order(size):
    if size == 16:
        chips = [(0, 0), (1, 0), (2, 0), (3, 0), (3, 1), (2, 1), (1, 1), (0, 1)]
        return [(x * 2 + y) * 2 + core for x, y in chips for core in (0, 1)]
    return list(range(size))


def per_device(src_codes, src_exps, signs, tgt_codes, tgt_exps):
    sources_bf = dequantize(src_codes, src_exps)
    targets_bf = dequantize(tgt_codes, tgt_exps)
    rhs_values = (2 * signs - 1).astype(jnp.bfloat16)
    source_sq = squares(sources_bf)
    cycle_size = lax.axis_size("blk")
    group_size = lax.axis_size("grp")
    block_rows = targets_bf.shape[0]
    half = block_rows // 2
    order = ring_order(cycle_size)
    forward = [(order[i], order[(i + 1) % cycle_size]) for i in range(cycle_size)]
    backward = [(b, a) for a, b in forward]

    def contribution(points_bf):
        return kernel_block(points_bf, sources_bf, source_sq, rhs_values)

    def halves(points_f, points_b):
        both = contribution(jnp.concatenate([points_f, points_b], axis=0))
        return both[:, :half], both[:, half:]

    def send(points_f, points_b):
        return lax.ppermute(points_f, "blk", forward), lax.ppermute(points_b, "blk", backward)

    def advance(counter, carried):
        points_f, points_b, sums_f, sums_b, part_f, part_b = carried
        sums_f, sums_b = send(sums_f + part_f, sums_b + part_b)
        next_f, next_b = send(points_f, points_b)
        part_f, part_b = halves(points_f, points_b)
        return (next_f, next_b, sums_f, sums_b, part_f, part_b)

    points_f, points_b = send(targets_bf[:half], targets_bf[half:])
    own = contribution(targets_bf)
    zeros = jnp.zeros_like(own[:, :half])
    carried = (points_f, points_b, zeros, zeros, own[:, :half], own[:, half:])
    carried = lax.fori_loop(0, cycle_size - 2, advance, carried)
    points_f, points_b, sums_f, sums_b, part_f, part_b = carried
    sums_f, sums_b = send(sums_f + part_f, sums_b + part_b)
    part_f, part_b = halves(points_f, points_b)
    complete = jnp.concatenate([sums_f + part_f, sums_b + part_b], axis=1)
    owned = exchange_scatter(complete, "grp")
    mine_f, mine_b = send(owned[:, :half], owned[:, half:])
    owned_sums = jnp.concatenate([mine_f, mine_b], axis=1)
    source_total = src_codes.shape[0] * group_size * cycle_size
    return owned_sums.T * (4.0 / math.sqrt(source_total))


def solution(mesh):
    placed = (
        P(("grp", "blk"), None),
        P(("grp", "blk"), None),
        P(("grp", "blk"), None),
        P("blk", None),
        P("blk", None),
    )
    return jax.shard_map(
        per_device, mesh=mesh, in_specs=placed, out_specs=P("blk", "grp"), check_vma=False
    )
```

```python
import math

import jax
import jax.numpy as jnp
from jax import lax
from jax.sharding import PartitionSpec as P

kernel_rate = 20.0


def shifted(block, axis, distance):
    devices = range(lax.axis_size(axis))
    route = [((i - distance) % len(devices), i) for i in devices]
    return lax.ppermute(block, axis, route)


def dequantize(codes, exponents):
    points, columns = codes.shape
    blocks = exponents.shape[1]
    factor = jnp.zeros(exponents.shape, jnp.float32)
    for level_index in range(4):
        factor = factor + jnp.where(exponents == level_index, 2.0 ** (level_index - 9), 0.0)
    scaled_codes = (
        codes.reshape(points, blocks, columns // blocks).astype(jnp.float32) * factor[:, :, None]
    )
    return scaled_codes.reshape(points, columns).astype(jnp.bfloat16)


def squares(points_bf):
    widened = points_bf.astype(jnp.float32)
    return jnp.sum(widened * widened, axis=1)


def kernel_block(targets_bf, sources_bf, source_sq, rhs_values):
    target_sq = squares(targets_bf)
    inner_products = lax.dot_general(
        targets_bf, sources_bf, (((1,), (1,)), ((), ())), preferred_element_type=jnp.float32
    )
    squared = target_sq[:, None] + source_sq[None, :] - 2.0 * inner_products
    scaled = kernel_rate * jnp.sqrt(squared) / math.sqrt(targets_bf.shape[1])
    matern = ((1.0 + scaled + scaled * scaled / 3.0) * jnp.exp(-scaled)).astype(jnp.bfloat16)
    return lax.dot_general(
        rhs_values, matern, (((0,), (1,)), ((), ())), preferred_element_type=jnp.float32
    )


def staged_scatter(sums, axis, inner=8):
    size = lax.axis_size(axis)
    outer = size // inner
    if size != outer * inner or outer < 2:
        return exchange_scatter(sums, axis)
    rows, cols = sums.shape
    chunk = rows // size
    pieces = sums.reshape(outer, inner, chunk, cols)
    near = [[o * inner + i for i in range(inner)] for o in range(outer)]
    pieces = lax.all_to_all(pieces, axis, 1, 1, axis_index_groups=near, tiled=True)
    pieces = jnp.sum(pieces.reshape(outer, inner, chunk, cols), axis=1)
    far = [[o * inner + i for o in range(outer)] for i in range(inner)]
    pieces = lax.all_to_all(pieces, axis, 0, 0, axis_index_groups=far, tiled=True)
    return jnp.sum(pieces, axis=0)


def exchange_scatter(sums, axis):
    size = lax.axis_size(axis)
    rows, cols = sums.shape
    pieces = sums.reshape(size, rows // size, cols)
    pieces = lax.all_to_all(pieces, axis, 0, 0, tiled=False)
    return jnp.sum(pieces, axis=0)


def halving_scatter(sums, axis):
    size = lax.axis_size(axis)
    me = lax.axis_index(axis)
    bits = size.bit_length() - 1
    rows, cols = sums.shape
    chunk = rows // size
    parts = sums.reshape((2,) * bits + (chunk, cols))
    order = [b for b in (0, 1, 3, 2) if b < bits] + [b for b in range(bits) if b not in (0, 1, 3, 2)]
    remaining = list(range(bits - 1, -1, -1))
    for bit in order:
        position = remaining.index(bit)
        mine = (me >> bit) & 1
        kept = lax.dynamic_index_in_dim(parts, mine, position, keepdims=False)
        sent = lax.dynamic_index_in_dim(parts, 1 - mine, position, keepdims=False)
        route = [(i, i ^ (1 << bit)) for i in range(size)]
        parts = kept + lax.ppermute(sent, axis, route)
        remaining.pop(position)
    return parts.reshape(chunk, cols)


def ring_order(size):
    if size == 16:
        chips = [(0, 0), (1, 0), (2, 0), (3, 0), (3, 1), (2, 1), (1, 1), (0, 1)]
        return [(x * 2 + y) * 2 + core for x, y in chips for core in (0, 1)]
    return list(range(size))


def per_device(src_codes, src_exps, signs, tgt_codes, tgt_exps):
    sources_bf = dequantize(src_codes, src_exps)
    targets_bf = dequantize(tgt_codes, tgt_exps)
    rhs_values = (2 * signs - 1).astype(jnp.bfloat16)
    source_sq = squares(sources_bf)
    cycle_size = lax.axis_size("blk")
    group_size = lax.axis_size("grp")
    block_rows = targets_bf.shape[0]
    half = block_rows // 2
    order = ring_order(cycle_size)
    forward = [(order[i], order[(i + 1) % cycle_size]) for i in range(cycle_size)]
    backward = [(b, a) for a, b in forward]

    def contribution(points_bf):
        return kernel_block(points_bf, sources_bf, source_sq, rhs_values)

    def halves(points_f, points_b):
        both = contribution(jnp.concatenate([points_f, points_b], axis=0))
        return both[:, :half], both[:, half:]

    def send(points_f, points_b):
        return lax.ppermute(points_f, "blk", forward), lax.ppermute(points_b, "blk", backward)

    def advance(counter, carried):
        points_f, points_b, sums_f, sums_b, part_f, part_b = carried
        sums_f, sums_b = send(sums_f + part_f, sums_b + part_b)
        next_f, next_b = send(points_f, points_b)
        part_f, part_b = halves(points_f, points_b)
        return (next_f, next_b, sums_f, sums_b, part_f, part_b)

    points_f, points_b = send(targets_bf[:half], targets_bf[half:])
    own = contribution(targets_bf)
    zeros = jnp.zeros_like(own[:, :half])
    carried = (points_f, points_b, zeros, zeros, own[:, :half], own[:, half:])
    carried = lax.fori_loop(0, cycle_size - 2, advance, carried)
    points_f, points_b, sums_f, sums_b, part_f, part_b = carried
    sums_f, sums_b = send(sums_f + part_f, sums_b + part_b)
    part_f, part_b = halves(points_f, points_b)
    complete = jnp.concatenate([sums_f + part_f, sums_b + part_b], axis=1)
    owned = staged_scatter(complete, "grp")
    mine_f, mine_b = send(owned[:, :half], owned[:, half:])
    owned_sums = jnp.concatenate([mine_f, mine_b], axis=1)
    source_total = src_codes.shape[0] * group_size * cycle_size
    return owned_sums.T * (4.0 / math.sqrt(source_total))


def solution(mesh):
    placed = (
        P(("grp", "blk"), None),
        P(("grp", "blk"), None),
        P(("grp", "blk"), None),
        P("blk", None),
        P("blk", None),
    )
    return jax.shard_map(
        per_device, mesh=mesh, in_specs=placed, out_specs=P("blk", "grp"), check_vma=False
    )
```

```python
import math

import jax
import jax.numpy as jnp
from jax import lax
from jax.sharding import PartitionSpec as P

kernel_rate = 20.0


def shifted(block, axis, distance):
    devices = range(lax.axis_size(axis))
    route = [((i - distance) % len(devices), i) for i in devices]
    return lax.ppermute(block, axis, route)


def dequantize(codes, exponents):
    points, columns = codes.shape
    blocks = exponents.shape[1]
    factor = jnp.zeros(exponents.shape, jnp.float32)
    for level_index in range(4):
        factor = factor + jnp.where(exponents == level_index, 2.0 ** (level_index - 9), 0.0)
    scaled_codes = (
        codes.reshape(points, blocks, columns // blocks).astype(jnp.bfloat16)
        * factor.astype(jnp.bfloat16)[:, :, None]
    )
    return scaled_codes.reshape(points, columns)


def squares(points_bf):
    widened = points_bf.astype(jnp.float32)
    return jnp.sum(widened * widened, axis=1)


def kernel_block(targets_bf, sources_bf, source_sq, rhs_values):
    target_sq = squares(targets_bf)
    inner_products = lax.dot_general(
        targets_bf, sources_bf, (((1,), (1,)), ((), ())), preferred_element_type=jnp.float32
    )
    squared = target_sq[:, None] + source_sq[None, :] - 2.0 * inner_products
    scaled = kernel_rate * jnp.sqrt(squared) / math.sqrt(targets_bf.shape[1])
    matern = ((1.0 + scaled + scaled * scaled / 3.0) * jnp.exp(-scaled)).astype(jnp.bfloat16)
    return lax.dot_general(
        rhs_values, matern, (((0,), (1,)), ((), ())), preferred_element_type=jnp.float32
    )


def exchange_scatter(sums, axis):
    size = lax.axis_size(axis)
    rows, cols = sums.shape
    pieces = sums.reshape(size, rows // size, cols)
    pieces = lax.all_to_all(pieces, axis, 0, 0, tiled=False)
    return jnp.sum(pieces, axis=0)


def halving_scatter(sums, axis):
    size = lax.axis_size(axis)
    me = lax.axis_index(axis)
    bits = size.bit_length() - 1
    rows, cols = sums.shape
    chunk = rows // size
    parts = sums.reshape((2,) * bits + (chunk, cols))
    order = [b for b in (0, 1, 3, 2) if b < bits] + [b for b in range(bits) if b not in (0, 1, 3, 2)]
    remaining = list(range(bits - 1, -1, -1))
    for bit in order:
        position = remaining.index(bit)
        mine = (me >> bit) & 1
        kept = lax.dynamic_index_in_dim(parts, mine, position, keepdims=False)
        sent = lax.dynamic_index_in_dim(parts, 1 - mine, position, keepdims=False)
        route = [(i, i ^ (1 << bit)) for i in range(size)]
        parts = kept + lax.ppermute(sent, axis, route)
        remaining.pop(position)
    return parts.reshape(chunk, cols)


def ring_order(size):
    if size == 16:
        chips = [(0, 0), (1, 0), (2, 0), (3, 0), (3, 1), (2, 1), (1, 1), (0, 1)]
        return [(x * 2 + y) * 2 + core for x, y in chips for core in (0, 1)]
    return list(range(size))


def per_device(src_codes, src_exps, signs, tgt_codes, tgt_exps):
    sources_bf = dequantize(src_codes, src_exps)
    targets_bf = dequantize(tgt_codes, tgt_exps)
    rhs_values = (2 * signs - 1).astype(jnp.bfloat16)
    source_sq = squares(sources_bf)
    cycle_size = lax.axis_size("blk")
    group_size = lax.axis_size("grp")
    block_rows = targets_bf.shape[0]
    half = block_rows // 2
    order = ring_order(cycle_size)
    forward = [(order[i], order[(i + 1) % cycle_size]) for i in range(cycle_size)]
    backward = [(b, a) for a, b in forward]

    def contribution(points_bf):
        return kernel_block(points_bf, sources_bf, source_sq, rhs_values)

    def halves(points_f, points_b):
        both = contribution(jnp.concatenate([points_f, points_b], axis=0))
        return both[:, :half], both[:, half:]

    def send(points_f, points_b):
        return lax.ppermute(points_f, "blk", forward), lax.ppermute(points_b, "blk", backward)

    def advance(counter, carried):
        points_f, points_b, sums_f, sums_b, part_f, part_b = carried
        sums_f, sums_b = send(sums_f + part_f, sums_b + part_b)
        next_f, next_b = send(points_f, points_b)
        part_f, part_b = halves(points_f, points_b)
        return (next_f, next_b, sums_f, sums_b, part_f, part_b)

    points_f, points_b = send(targets_bf[:half], targets_bf[half:])
    own = contribution(targets_bf)
    zeros = jnp.zeros_like(own[:, :half])
    carried = (points_f, points_b, zeros, zeros, own[:, :half], own[:, half:])
    carried = lax.fori_loop(0, cycle_size - 2, advance, carried)
    points_f, points_b, sums_f, sums_b, part_f, part_b = carried
    sums_f, sums_b = send(sums_f + part_f, sums_b + part_b)
    part_f, part_b = halves(points_f, points_b)
    complete = jnp.concatenate([sums_f + part_f, sums_b + part_b], axis=1)
    owned = exchange_scatter(complete, "grp")
    mine_f, mine_b = send(owned[:, :half], owned[:, half:])
    owned_sums = jnp.concatenate([mine_f, mine_b], axis=1)
    source_total = src_codes.shape[0] * group_size * cycle_size
    return owned_sums.T * (4.0 / math.sqrt(source_total))


def solution(mesh):
    placed = (
        P(("grp", "blk"), None),
        P(("grp", "blk"), None),
        P(("grp", "blk"), None),
        P("blk", None),
        P("blk", None),
    )
    return jax.shard_map(
        per_device, mesh=mesh, in_specs=placed, out_specs=P("blk", "grp"), check_vma=False
    )
```
